128 devices in a mesh: row: 8 (over x, core), col: 16 (over z, y).
Axes of the slice: x: 4, y: 4, z: 4, core: 2. Of those that a mesh axis runs over, the one named last changes fastest.
Arguments:
- hidden: bfloat16 [2048, 3584], P(('row', 'col')), may hold values from -6 to 6
- route_ids: int32 [2048, 8], P(('row', 'col')), may hold values from 0 to 127, all different within a row; in each aligned block of 16 rows (0 to 15, 16 to 31, ...) at most 2 rows name the same one
- route_scores: float32 [2048, 8], P(('row', 'col')), may hold values from 0.05 to 1
- gate_weight: bfloat16 [128, 3584, 1024], P(('row', 'col')), may hold values from -0.09375 to 0.09375
- up_weight: bfloat16 [128, 3584, 1024], P(('row', 'col')), may hold values from -0.09375 to 0.09375
- down_weight: bfloat16 [128, 1024, 3584], P(('row', 'col')), may hold values from -0.1875 to 0.1875
- queries: bfloat16 [2048, 64, 576], P(('row', 'col'))
- latent_cache: bfloat16 [2048, 128, 576], P(('row', 'col'))
- lengths: int32 [2048], P(('row', 'col')), may hold values from 1 to 128, 131072 in all
Outputs:
- expert_mix: bfloat16 [2048, 3584], P(('row', 'col'))
- context: bfloat16 [2048, 64, 512], P(('row', 'col'))
The draws below stay inside these ranges and needn't reach their ends.
Inputs may be any that keep to these rules, and one draw needn't show every extreme that they name: `route_ids`: among the 16 sequences of one device (aligned blocks of rows), no expert is named more than 2 times, and in every draw some expert is named exactly 2 times; each row names 8 different experts. `lengths`: some sequence fills all 128 slots.
All inputs are finite; a program needn't handle non-finite values. No bound on the sum of `lengths` on one device may be relied on, other than what follows from the above.
Results may differ from the reference program's by a relative error of at most 0.013.
Values may be sent and summed in bfloat16 or wider, within the bound.
No kernel may reach another device: no remote copies, remote signals or barrier semaphores. Data moves between devices by JAX's collectives and lax.ppermute only.
A program may use at most 128 MiB of HBM per device.

```python
import math
import jax
import jax.numpy as jnp
import numpy as np
from jax import lax

D = 3584
FF = 1024
HEADS = 64
LATENT = 512
ROPE = 64
CACHE = 128
TOP = 8
SEQ_DEV = 16
SEQS = 2048
EXPERTS = 128
CAP = 2


def draw_queries(key, part):
    shape = (SEQS, HEADS, LATENT + ROPE)
    values = jax.random.normal(jax.random.fold_in(key, 21), shape, jnp.float32)
    return values.astype(jnp.bfloat16)


def draw_latent_cache(key, part):
    shape = (SEQS, CACHE, LATENT + ROPE)
    values = jax.random.normal(jax.random.fold_in(key, 31), shape, jnp.float32)
    return values.astype(jnp.bfloat16)


def levels(rng, extent, pieces, low, top_value):
    level, own = 1.0, jax.random.fold_in(rng, 6)
    for dim, parts in pieces:
        heights = jnp.exp(jax.random.uniform(jax.random.fold_in(own, dim), (parts,), jnp.float32, low / len(pieces), top_value / len(pieces)))
        level = level * jnp.repeat(heights, extent[dim] // parts).reshape([-1 if axis == dim else 1 for axis in range(len(extent))])
    return level


def length_profile(amount, total, limit, slope):
    portions = [(1 << 20) // math.isqrt(standing ** slope) + 1 for standing in range(2, amount + 1)]
    surplus, given = total - limit - (amount - 1), [1] * (amount - 1)
    while surplus > 0:
        candidates = [i for i in range(amount - 1) if given[i] < limit]
        pool, left = sum([portions[i] for i in candidates]), surplus
        for i in candidates:
            extra = min(limit - given[i], max(1, left * portions[i] // pool), surplus)
            given[i] = given[i] + extra
            surplus = surplus - extra
    return np.array([limit] + given)


def ragged_sizes(own_key, count, total, limit, slope):
    if count == 2:
        one = jax.random.randint(own_key, (), max(1, total - limit), min(limit, total - 1) + 1)
        return jnp.stack([one, total - one])
    sizes = jnp.asarray(length_profile(count, total, limit, slope), jnp.int32)
    pairs = (count - 1) // 2
    donor, sink = sizes[1:1 + 2 * pairs:2], sizes[2:2 + 2 * pairs:2]
    margin = jnp.minimum(donor - 1, limit - sink)
    passed = jax.random.randint(jax.random.fold_in(own_key, 1), (pairs,), 0, 1 << 20) % (margin + 1)
    sizes = sizes.at[1:1 + 2 * pairs:2].set(donor - passed).at[2:2 + 2 * pairs:2].set(sink + passed)
    return sizes[jax.random.permutation(jax.random.fold_in(own_key, 2), count)]


def routed_block(stream_key, own, number, rows, number_of, top, most, lean):
    order = jax.random.permutation(stream_key, number_of)
    crowded, common = portions_of(number_of, rows * top, most, lean, True), portions_of(number_of, rows * top, most, lean, False)
    places = jnp.arange(number_of)

    def named(tallies, turn):
        used = int((tallies > 0).sum())
        fixed = max(1, used // 4)
        shifted = fixed + (places - fixed + turn * (used - fixed)) % max(1, number_of - fixed)
        return jnp.zeros((number_of,), jnp.int32).at[order[jnp.where(places < fixed, places, shifted)]].set(jnp.asarray(tallies, jnp.int32))

    tallies = jnp.where(number % 4 == 0, named(crowded, number // 4), named(common, number - number // 4 - 1))
    mixed = jax.random.permutation(jax.random.fold_in(own, 3), number_of)
    donor, taker = mixed[0:number_of // 2 * 2:2], mixed[1:number_of // 2 * 2:2]
    margin = jnp.minimum(tallies[donor] - 1, most - tallies[taker]) // 2
    margin = jnp.where((donor == order[0]) | (taker == order[0]) | (tallies[taker] == 0), 0, jnp.maximum(margin, 0))
    shifted = jax.random.randint(jax.random.fold_in(own, 4), (number_of // 2,), 0, 1 << 20) % (margin + 1)
    tallies = tallies.at[donor].add(-shifted).at[taker].add(shifted)
    items = jnp.searchsorted(jnp.cumsum(tallies), jnp.arange(rows * top), side="right").astype(jnp.int32)
    listing = items.reshape(top, rows).T
    listing = listing[jax.random.permutation(jax.random.fold_in(own, 1), rows)]
    turn = jax.random.randint(jax.random.fold_in(own, 2), (rows, 1), 0, top)
    return jnp.take_along_axis(listing, (jnp.arange(top)[None, :] + turn) % top, axis=1)


def portions_of(count, total, limit, lean, full):
    portions = [(1 << 20) // math.isqrt(grade ** lean) + 1 for grade in range(1, count + 1)]
    largest = limit if full else min(limit, max(-(-total // count), total * portions[0] // sum(portions)))
    least = 1 if total - largest >= count - 1 else 0
    holding, spare = [largest] + [least] * (count - 1), total - largest - least * (count - 1)
    while spare > 0:
        free = [i for i in range(1, count) if holding[i] < largest] or [i for i in range(1, count) if holding[i] < limit]
        pool, budget = sum([portions[i] for i in free]), spare
        for i in free:
            extra = min(limit - holding[i], max(1, budget * portions[i] // pool), spare)
            holding[i] = holding[i] + extra
            spare = spare - extra
    return np.array(holding)


def noise(stream_key, shape, scale, bound, split=(), kind=jnp.bfloat16):
    loudness = levels(stream_key, shape, split, -0.22, 0.18) if split else 1.0
    entries = jax.random.normal(stream_key, shape, jnp.float32) * scale * loudness
    return jnp.minimum(jnp.maximum(entries, -bound), bound).astype(kind)


def setup_inputs(seed: int = 0) -> dict:
    splits = jax.random.split(jax.random.key(seed), 10)
    hidden = noise(splits[0], (SEQS, D), 1.0, 6.0, ((0, 128),))
    route_ids_keys = jax.random.split(jax.random.fold_in(splits[1], 1), SEQS // SEQ_DEV)
    route_ids_turns = jax.random.permutation(jax.random.fold_in(splits[1], 3), SEQS // SEQ_DEV)
    route_ids = jax.vmap(lambda own, number: routed_block(jax.random.fold_in(splits[1], 2), own, number, SEQ_DEV, EXPERTS, TOP, CAP, 2))(route_ids_keys, route_ids_turns).reshape((SEQS, TOP))
    route_scores = jnp.clip(0.05 + 0.95 * jax.random.uniform(splits[2], (SEQS, TOP), jnp.float32) ** levels(splits[2], (SEQS, TOP), ((0, 128),), -0.2, 0.2), 0.05, 1.0)
    gate_weight = noise(splits[3], (EXPERTS, D, FF), D ** -0.5, 0.09375, ((0, 128),))
    up_weight = noise(splits[4], (EXPERTS, D, FF), D ** -0.5, 0.09375, ((0, 128),))
    down_weight = noise(splits[5], (EXPERTS, FF, D), FF ** -0.5, 0.1875, ((0, 128),))
    queries = draw_queries(jax.random.fold_in(splits[9], 71), 0)
    latent_cache = draw_latent_cache(jax.random.fold_in(splits[9], 71), 0)
    lengths = ragged_sizes(splits[8], SEQS, SEQS * CACHE // 2, CACHE, 2).astype(jnp.int32)
    return dict(hidden=hidden, route_ids=route_ids, route_scores=route_scores, gate_weight=gate_weight, up_weight=up_weight, down_weight=down_weight, queries=queries, latent_cache=latent_cache, lengths=lengths)


SOFTMAX_SCALE = 192 ** -0.5


def attention(queries, latent_cache, lengths):
    query_f = queries.astype(jnp.float32)
    cache_f = latent_cache.astype(jnp.float32)
    scores = jnp.einsum("shc,slc->shl", query_f, cache_f) * SOFTMAX_SCALE
    visible = jnp.arange(CACHE, dtype=jnp.int32)[None, None, :] < lengths[:, None, None]
    scores = jnp.where(visible, scores, jnp.float32(-1e30))
    row_max = jnp.max(scores, axis=-1, keepdims=True)
    numer = jnp.where(visible, jnp.exp(scores - row_max), jnp.float32(0.0))
    probabilities = (numer / jnp.sum(numer, axis=-1, keepdims=True)).astype(jnp.bfloat16)
    context = jnp.einsum("shl,slc->shc", probabilities.astype(jnp.float32), cache_f[:, :, :LATENT])
    return context.astype(jnp.bfloat16)


def expert_block(operands):
    buffer, w_gate, w_up, w_down = operands
    gate_part = jnp.dot(buffer, w_gate, preferred_element_type=jnp.float32)
    up_part = jnp.dot(buffer, w_up, preferred_element_type=jnp.float32)
    units = (jax.nn.silu(gate_part) * up_part).astype(jnp.bfloat16)
    return jnp.dot(units, w_down, preferred_element_type=jnp.float32).astype(jnp.bfloat16)


def reference(hidden, route_ids, route_scores, gate_weight, up_weight, down_weight, queries, latent_cache, lengths):
    combine = 2.5 * route_scores / jnp.sum(route_scores, axis=-1, keepdims=True)
    flat_ids = route_ids.reshape(-1).astype(jnp.int32)
    onehot = (flat_ids[:, None] == jnp.arange(EXPERTS, dtype=jnp.int32)[None, :]).astype(jnp.int32)
    blocks = onehot.reshape(EXPERTS, SEQ_DEV * TOP, EXPERTS)
    before = jnp.cumsum(blocks, axis=1) - blocks
    ranking = jnp.sum(before * blocks, axis=-1).reshape(-1).astype(jnp.int32)
    source = (jnp.arange(SEQS * TOP, dtype=jnp.int32) // (SEQ_DEV * TOP)).astype(jnp.int32)
    position = (source * CAP + ranking).astype(jnp.int32)
    token_of = (jnp.arange(SEQS * TOP, dtype=jnp.int32) // TOP).astype(jnp.int32)
    buffers = jnp.zeros((EXPERTS, EXPERTS * CAP, D), jnp.bfloat16).at[flat_ids, position].set(hidden[token_of])
    outputs = lax.map(expert_block, (buffers, gate_weight, up_weight, down_weight))
    picked = outputs[flat_ids, position].astype(jnp.float32).reshape(SEQS, TOP, D)
    expert_mix = jnp.sum(picked * combine[:, :, None], axis=1).astype(jnp.bfloat16)
    context = attention(queries, latent_cache, lengths)
    return (expert_mix, context)
```

```python
import jax
import jax.numpy as jnp
from jax import lax
from jax.experimental import pallas as pl
from jax.experimental.pallas import tpu as pltpu
from jax.sharding import PartitionSpec as P

LATENT = 512


SOFTMAX_SCALE = 192 ** (-0.5)


def attention(queries, latent_cache, lengths):
    scores = (
        jnp.einsum("shc,slc->shl", queries, latent_cache, preferred_element_type=jnp.float32)
        * SOFTMAX_SCALE
    )
    visible = (
        jnp.arange(latent_cache.shape[1], dtype=jnp.int32)[None, None, :] < lengths[:, None, None]
    )
    scores = jnp.where(visible, scores, jnp.float32(-1e30))
    row_max = jnp.max(scores, axis=-1, keepdims=True)
    numer = jnp.where(visible, jnp.exp(scores - row_max), jnp.float32(0.0))
    probabilities = (numer / jnp.sum(numer, axis=-1, keepdims=True)).astype(jnp.bfloat16)
    context = jnp.einsum(
        "shl,slc->shc",
        probabilities,
        latent_cache[:, :, :LATENT],
        preferred_element_type=jnp.float32,
    )
    return context.astype(jnp.bfloat16)


FF_BLOCK = 256


def expert_kernel(rows_ref, gate_ref, up_ref, down_ref, out_ref, acc_ref):
    step = pl.program_id(0)

    @pl.when(step == 0)
    def _():
        acc_ref[...] = jnp.zeros_like(acc_ref)

    rows = rows_ref[...]
    gate_part = jnp.dot(rows, gate_ref[...], preferred_element_type=jnp.float32)
    up_part = jnp.dot(rows, up_ref[...], preferred_element_type=jnp.float32)
    units = (gate_part / (1.0 + jnp.exp(-gate_part)) * up_part).astype(jnp.bfloat16)
    acc_ref[...] += jnp.dot(units, down_ref[...], preferred_element_type=jnp.float32)

    @pl.when(step == pl.num_programs(0) - 1)
    def _():
        out_ref[...] = acc_ref[...].astype(out_ref.dtype)


def expert_rows(buffer, gate_weight, up_weight, down_weight):
    model_width = buffer.shape[-1]
    hidden_units = gate_weight.shape[-1]
    row_block = buffer.reshape(-1, model_width)
    row_count = row_block.shape[0]
    result = pl.pallas_call(
        expert_kernel,
        grid=(hidden_units // FF_BLOCK,),
        in_specs=[
            pl.BlockSpec((row_count, model_width), lambda f: (0, 0)),
            pl.BlockSpec((None, model_width, FF_BLOCK), lambda f: (0, 0, f)),
            pl.BlockSpec((None, model_width, FF_BLOCK), lambda f: (0, 0, f)),
            pl.BlockSpec((None, FF_BLOCK, model_width), lambda f: (0, f, 0)),
        ],
        out_specs=pl.BlockSpec((row_count, model_width), lambda f: (0, 0)),
        out_shape=jax.ShapeDtypeStruct((row_count, model_width), jnp.bfloat16),
        scratch_shapes=[pltpu.VMEM((row_count, model_width), jnp.float32)],
        compiler_params=pltpu.CompilerParams(
            dimension_semantics=("arbitrary",), vmem_limit_bytes=48 * 1024 * 1024
        ),
    )(row_block, gate_weight, up_weight, down_weight)
    return result.reshape(buffer.shape)


def slot_tables(targets, token_count, top_count, slot_count, hidden_rows, weights):
    placed = targets[:, None] == jnp.arange(slot_count, dtype=jnp.int32)[None, :]
    share = placed.reshape(token_count, top_count, slot_count)
    layout = jnp.any(share, axis=1).astype(jnp.bfloat16)
    outgoing = lax.dot_general(
        layout, hidden_rows, (((0,), (0,)), ((), ())), preferred_element_type=jnp.float32
    )
    mixing = jnp.sum(share.astype(jnp.float32) * weights[:, :, None], axis=1)
    return (outgoing.astype(jnp.bfloat16), mixing)


def shards(
    hidden,
    route_ids,
    route_scores,
    gate_weight,
    up_weight,
    down_weight,
    queries,
    latent_cache,
    lengths,
):
    seq_dev, model_width = hidden.shape
    top_count = route_ids.shape[1]
    row_count = lax.axis_size("row")
    col_count = lax.axis_size("col")
    experts = row_count * col_count
    capacity = max(2, 2 * seq_dev * top_count // experts)
    slot_count = experts * capacity
    combine = 2.5 * route_scores / jnp.sum(route_scores, axis=-1, keepdims=True)
    flat_ids = route_ids.reshape(-1)
    onehot = (flat_ids[:, None] == jnp.arange(experts, dtype=jnp.int32)[None, :]).astype(jnp.int32)
    before = jnp.cumsum(onehot, axis=0) - onehot
    ranking = jnp.sum(before * onehot, axis=1)
    targets = flat_ids * capacity + ranking
    outgoing, mixing = slot_tables(targets, seq_dev, top_count, slot_count, hidden, combine)
    outgoing = outgoing.reshape(experts, capacity, model_width)
    computed = expert_rows(
        lax.all_to_all(outgoing, ("row", "col"), split_axis=0, concat_axis=0, tiled=True),
        gate_weight,
        up_weight,
        down_weight,
    )
    returned = lax.all_to_all(computed, ("row", "col"), split_axis=0, concat_axis=0, tiled=True)
    returned = returned.reshape(slot_count, model_width)
    mixture = jnp.dot(
        mixing,
        returned.astype(jnp.float32),
        precision=lax.Precision.HIGHEST,
        preferred_element_type=jnp.float32,
    )
    context = attention(queries, latent_cache, lengths)
    return (mixture.astype(jnp.bfloat16), context)


def solution(mesh):
    placed = (
        P(("row", "col"), None),
        P(("row", "col"), None),
        P(("row", "col"), None),
        P(("row", "col"), None, None),
        P(("row", "col"), None, None),
        P(("row", "col"), None, None),
        P(("row", "col"), None, None),
        P(("row", "col"), None, None),
        P(("row", "col")),
    )
    return jax.shard_map(
        shards,
        mesh=mesh,
        in_specs=placed,
        out_specs=(P(("row", "col"), None), P(("row", "col"), None, None)),
        check_vma=False,
    )
```

```python
import jax
import jax.numpy as jnp
from jax import lax
from jax.experimental import pallas as pl
from jax.experimental.pallas import tpu as pltpu
from jax.sharding import PartitionSpec as P

LATENT = 512


SOFTMAX_SCALE = 192 ** (-0.5)


def attention(queries, latent_cache, lengths):
    scores = (
        jnp.einsum("shc,slc->shl", queries, latent_cache, preferred_element_type=jnp.float32)
        * SOFTMAX_SCALE
    )
    visible = (
        jnp.arange(latent_cache.shape[1], dtype=jnp.int32)[None, None, :] < lengths[:, None, None]
    )
    scores = jnp.where(visible, scores, jnp.float32(-1e30))
    row_max = jnp.max(scores, axis=-1, keepdims=True)
    numer = jnp.where(visible, jnp.exp(scores - row_max), jnp.float32(0.0))
    probabilities = (numer / jnp.sum(numer, axis=-1, keepdims=True)).astype(jnp.bfloat16)
    context = jnp.einsum(
        "shl,slc->shc",
        probabilities,
        latent_cache[:, :, :LATENT],
        preferred_element_type=jnp.float32,
    )
    return context.astype(jnp.bfloat16)


FF_BLOCK = 256


def expert_kernel(rows_ref, gate_ref, up_ref, down_ref, out_ref, acc_ref):
    step = pl.program_id(0)
    capacity = rows_ref.shape[1]
    sources = rows_ref.shape[0]

    @pl.when(step == 0)
    def _():
        acc_ref[...] = jnp.zeros_like(acc_ref)

    for slot in range(capacity):
        rows = rows_ref[:, slot, :]
        gate_part = jnp.dot(rows, gate_ref[...], preferred_element_type=jnp.float32)
        up_part = jnp.dot(rows, up_ref[...], preferred_element_type=jnp.float32)
        units = (gate_part / (1.0 + jnp.exp(-gate_part)) * up_part).astype(jnp.bfloat16)
        acc_ref[slot] += jnp.dot(units, down_ref[...], preferred_element_type=jnp.float32)

    @pl.when(step == pl.num_programs(0) - 1)
    def _():
        for slot in range(capacity):
            out_ref[:, slot, :] = acc_ref[slot].astype(out_ref.dtype)


def expert_rows(buffer, gate_weight, up_weight, down_weight):
    sources, capacity, model_width = buffer.shape
    hidden_units = gate_weight.shape[-1]
    return pl.pallas_call(
        expert_kernel,
        grid=(hidden_units // FF_BLOCK,),
        in_specs=[
            pl.BlockSpec(buffer.shape, lambda f: (0, 0, 0)),
            pl.BlockSpec((None, model_width, FF_BLOCK), lambda f: (0, 0, f)),
            pl.BlockSpec((None, model_width, FF_BLOCK), lambda f: (0, 0, f)),
            pl.BlockSpec((None, FF_BLOCK, model_width), lambda f: (0, f, 0)),
        ],
        out_specs=pl.BlockSpec(buffer.shape, lambda f: (0, 0, 0)),
        out_shape=jax.ShapeDtypeStruct(buffer.shape, jnp.bfloat16),
        scratch_shapes=[pltpu.VMEM((capacity, sources, model_width), jnp.float32)],
        compiler_params=pltpu.CompilerParams(
            dimension_semantics=("arbitrary",), vmem_limit_bytes=48 * 1024 * 1024
        ),
    )(buffer, gate_weight, up_weight, down_weight)


def dispatch_kernel(layout_ref, hidden_ref, out_ref):
    hidden_rows = hidden_ref[...]
    for slot in range(out_ref.shape[1]):
        placed = jnp.dot(layout_ref[slot], hidden_rows, preferred_element_type=jnp.float32)
        out_ref[:, slot, :] = placed.astype(out_ref.dtype)


def combine_kernel(mixing_ref, returned_ref, out_ref):
    total = jnp.zeros(out_ref.shape, jnp.float32)
    for slot in range(returned_ref.shape[1]):
        rows = returned_ref[:, slot, :]
        weights = mixing_ref[slot]
        high = weights.astype(jnp.bfloat16)
        rest = weights - high.astype(jnp.float32)
        middle = rest.astype(jnp.bfloat16)
        low = (rest - middle.astype(jnp.float32)).astype(jnp.bfloat16)
        for part in (high, middle, low):
            total += jnp.dot(part, rows, preferred_element_type=jnp.float32)
    out_ref[...] = total.astype(out_ref.dtype)


def shards(
    hidden,
    route_ids,
    route_scores,
    gate_weight,
    up_weight,
    down_weight,
    queries,
    latent_cache,
    lengths,
):
    seq_dev, model_width = hidden.shape
    top_count = route_ids.shape[1]
    row_count = lax.axis_size("row")
    col_count = lax.axis_size("col")
    experts = row_count * col_count
    capacity = max(2, 2 * seq_dev * top_count // experts)
    combine = 2.5 * route_scores / jnp.sum(route_scores, axis=-1, keepdims=True)
    flat_ids = route_ids.reshape(-1)
    onehot = (flat_ids[:, None] == jnp.arange(experts, dtype=jnp.int32)[None, :]).astype(jnp.int32)
    before = jnp.cumsum(onehot, axis=0) - onehot
    ranking = jnp.sum(before * onehot, axis=1)
    share = (
        (onehot[None, :, :] > 0)
        & (ranking[None, :, None] == jnp.arange(capacity, dtype=jnp.int32)[:, None, None])
    ).reshape(capacity, seq_dev, top_count, experts)
    layout = jnp.swapaxes(jnp.any(share, axis=2), 1, 2).astype(jnp.bfloat16)
    mixing = jnp.sum(share.astype(jnp.float32) * combine[None, :, :, None], axis=2)
    outgoing = pl.pallas_call(
        dispatch_kernel,
        out_shape=jax.ShapeDtypeStruct((experts, capacity, model_width), jnp.bfloat16),
    )(layout, hidden)
    computed = expert_rows(
        lax.all_to_all(outgoing, ("row", "col"), split_axis=0, concat_axis=0, tiled=True),
        gate_weight,
        up_weight,
        down_weight,
    )
    returned = lax.all_to_all(computed, ("row", "col"), split_axis=0, concat_axis=0, tiled=True)
    mixture = pl.pallas_call(
        combine_kernel,
        out_shape=jax.ShapeDtypeStruct((seq_dev, model_width), jnp.bfloat16),
    )(mixing, returned)
    context = attention(queries, latent_cache, lengths)
    return (mixture, context)


def solution(mesh):
    placed = (
        P(("row", "col"), None),
        P(("row", "col"), None),
        P(("row", "col"), None),
        P(("row", "col"), None, None),
        P(("row", "col"), None, None),
        P(("row", "col"), None, None),
        P(("row", "col"), None, None),
        P(("row", "col"), None, None),
        P(("row", "col")),
    )
    return jax.shard_map(
        shards,
        mesh=mesh,
        in_specs=placed,
        out_specs=(P(("row", "col"), None), P(("row", "col"), None, None)),
        check_vma=False,
    )
```

```python
import jax
import jax.numpy as jnp
from jax import lax
from jax.experimental import pallas as pl
from jax.experimental.pallas import tpu as pltpu
from jax.sharding import PartitionSpec as P

LATENT = 512


SOFTMAX_SCALE = 192 ** (-0.5)


def attention(queries, latent_cache, lengths):
    scores = (
        jnp.einsum("shc,slc->shl", queries, latent_cache, preferred_element_type=jnp.float32)
        * SOFTMAX_SCALE
    )
    visible = (
        jnp.arange(latent_cache.shape[1], dtype=jnp.int32)[None, None, :] < lengths[:, None, None]
    )
    scores = jnp.where(visible, scores, jnp.float32(-1e30))
    row_max = jnp.max(scores, axis=-1, keepdims=True)
    numer = jnp.where(visible, jnp.exp(scores - row_max), jnp.float32(0.0))
    probabilities = (numer / jnp.sum(numer, axis=-1, keepdims=True)).astype(jnp.bfloat16)
    context = jnp.einsum(
        "shl,slc->shc",
        probabilities,
        latent_cache[:, :, :LATENT],
        preferred_element_type=jnp.float32,
    )
    return context.astype(jnp.bfloat16)


FF_BLOCK = 256


def expert_kernel(rows_ref, gate_ref, up_ref, down_ref, out_ref, slots_ref, acc_ref):
    step = pl.program_id(0)
    capacity = rows_ref.shape[1]

    @pl.when(step == 0)
    def _():
        for slot in range(capacity):
            slots_ref[slot] = rows_ref[:, slot, :]
        acc_ref[...] = jnp.zeros_like(acc_ref)

    for slot in range(capacity):
        rows = slots_ref[slot]
        gate_part = jnp.dot(rows, gate_ref[...], preferred_element_type=jnp.float32)
        up_part = jnp.dot(rows, up_ref[...], preferred_element_type=jnp.float32)
        units = (gate_part / (1.0 + jnp.exp(-gate_part)) * up_part).astype(jnp.bfloat16)
        acc_ref[slot] += jnp.dot(units, down_ref[...], preferred_element_type=jnp.float32)

    @pl.when(step == pl.num_programs(0) - 1)
    def _():
        for slot in range(capacity):
            out_ref[:, slot, :] = acc_ref[slot].astype(out_ref.dtype)


def expert_rows(buffer, gate_weight, up_weight, down_weight):
    sources, capacity, model_width = buffer.shape
    hidden_units = gate_weight.shape[-1]
    return pl.pallas_call(
        expert_kernel,
        grid=(hidden_units // FF_BLOCK,),
        in_specs=[
            pl.BlockSpec(buffer.shape, lambda f: (0, 0, 0)),
            pl.BlockSpec((None, model_width, FF_BLOCK), lambda f: (0, 0, f)),
            pl.BlockSpec((None, model_width, FF_BLOCK), lambda f: (0, 0, f)),
            pl.BlockSpec((None, FF_BLOCK, model_width), lambda f: (0, f, 0)),
        ],
        out_specs=pl.BlockSpec(buffer.shape, lambda f: (0, 0, 0)),
        out_shape=jax.ShapeDtypeStruct(buffer.shape, jnp.bfloat16),
        scratch_shapes=[
            pltpu.VMEM((capacity, sources, model_width), jnp.bfloat16),
            pltpu.VMEM((capacity, sources, model_width), jnp.float32),
        ],
        compiler_params=pltpu.CompilerParams(
            dimension_semantics=("arbitrary",), vmem_limit_bytes=48 * 1024 * 1024
        ),
    )(buffer, gate_weight, up_weight, down_weight)


def dispatch_kernel(layout_ref, hidden_ref, out_ref):
    hidden_rows = hidden_ref[...]
    for slot in range(out_ref.shape[1]):
        placed = jnp.dot(layout_ref[slot], hidden_rows, preferred_element_type=jnp.float32)
        out_ref[:, slot, :] = placed.astype(out_ref.dtype)


def shards(
    hidden,
    route_ids,
    route_scores,
    gate_weight,
    up_weight,
    down_weight,
    queries,
    latent_cache,
    lengths,
):
    seq_dev, model_width = hidden.shape
    top_count = route_ids.shape[1]
    row_count = lax.axis_size("row")
    col_count = lax.axis_size("col")
    experts = row_count * col_count
    capacity = max(2, 2 * seq_dev * top_count // experts)
    combine = 2.5 * route_scores / jnp.sum(route_scores, axis=-1, keepdims=True)
    flat_ids = route_ids.reshape(-1)
    onehot = (flat_ids[:, None] == jnp.arange(experts, dtype=jnp.int32)[None, :]).astype(jnp.int32)
    before = jnp.cumsum(onehot, axis=0) - onehot
    ranking = jnp.sum(before * onehot, axis=1)
    share = (
        (onehot[None, :, :] > 0)
        & (ranking[None, :, None] == jnp.arange(capacity, dtype=jnp.int32)[:, None, None])
    ).reshape(capacity, seq_dev, top_count, experts)
    layout = jnp.swapaxes(jnp.any(share, axis=2), 1, 2).astype(jnp.bfloat16)
    mixing = jnp.sum(share.astype(jnp.float32) * combine[None, :, :, None], axis=2)
    outgoing = pl.pallas_call(
        dispatch_kernel,
        out_shape=jax.ShapeDtypeStruct((experts, capacity, model_width), jnp.bfloat16),
    )(layout, hidden)
    computed = expert_rows(
        lax.all_to_all(outgoing, ("row", "col"), split_axis=0, concat_axis=0, tiled=True),
        gate_weight,
        up_weight,
        down_weight,
    )
    returned = lax.all_to_all(computed, ("row", "col"), split_axis=0, concat_axis=0, tiled=True)
    mixing = jnp.transpose(mixing, (1, 2, 0)).reshape(seq_dev, experts * capacity)
    returned = returned.reshape(experts * capacity, model_width)
    mixture = jnp.dot(
        mixing,
        returned.astype(jnp.float32),
        precision=lax.Precision.HIGHEST,
        preferred_element_type=jnp.float32,
    ).astype(jnp.bfloat16)
    context = attention(queries, latent_cache, lengths)
    return (mixture, context)


def solution(mesh):
    placed = (
        P(("row", "col"), None),
        P(("row", "col"), None),
        P(("row", "col"), None),
        P(("row", "col"), None, None),
        P(("row", "col"), None, None),
        P(("row", "col"), None, None),
        P(("row", "col"), None, None),
        P(("row", "col"), None, None),
        P(("row", "col")),
    )
    return jax.shard_map(
        shards,
        mesh=mesh,
        in_specs=placed,
        out_specs=(P(("row", "col"), None), P(("row", "col"), None, None)),
        check_vma=False,
    )
```

```python
import jax
import jax.numpy as jnp
from jax import lax
from jax.experimental import pallas as pl
from jax.experimental.pallas import tpu as pltpu
from jax.sharding import PartitionSpec as P

LATENT = 512


SOFTMAX_SCALE = 192 ** (-0.5)


def attention(queries, latent_cache, lengths):
    scores = (
        jnp.einsum("shc,slc->shl", queries, latent_cache, preferred_element_type=jnp.float32)
        * SOFTMAX_SCALE
    )
    visible = (
        jnp.arange(latent_cache.shape[1], dtype=jnp.int32)[None, None, :] < lengths[:, None, None]
    )
    scores = jnp.where(visible, scores, jnp.float32(-1e30))
    row_max = jnp.max(scores, axis=-1, keepdims=True)
    numer = jnp.where(visible, jnp.exp(scores - row_max), jnp.float32(0.0))
    probabilities = (numer / jnp.sum(numer, axis=-1, keepdims=True)).astype(jnp.bfloat16)
    context = jnp.einsum(
        "shl,slc->shc",
        probabilities,
        latent_cache[:, :, :LATENT],
        preferred_element_type=jnp.float32,
    )
    return context.astype(jnp.bfloat16)


FF_BLOCK = 512


def expert_kernel(rows_ref, gate_hbm, up_hbm, down_hbm, out_ref,
                  gate_vmem, up_vmem, down_vmem, slots_ref, acc_ref, sems):
    capacity = rows_ref.shape[1]
    blocks = gate_vmem.shape[-1] // FF_BLOCK
    copies = []
    for block in range(blocks):
        cols = pl.ds(block * FF_BLOCK, FF_BLOCK)
        trio = (
            pltpu.make_async_copy(gate_hbm.at[0, :, cols], gate_vmem.at[:, cols], sems.at[0, block]),
            pltpu.make_async_copy(up_hbm.at[0, :, cols], up_vmem.at[:, cols], sems.at[1, block]),
            pltpu.make_async_copy(down_hbm.at[0, cols, :], down_vmem.at[cols, :], sems.at[2, block]),
        )
        for copy in trio:
            copy.start()
        copies.append(trio)
    for slot in range(capacity):
        slots_ref[slot] = rows_ref[:, slot, :]
    for block in range(blocks):
        cols = pl.ds(block * FF_BLOCK, FF_BLOCK)
        gate_copy, up_copy, down_copy = copies[block]
        gate_copy.wait()
        up_copy.wait()
        down_copy.wait()
        for slot in range(capacity):
            rows = slots_ref[slot]
            gate_part = jnp.dot(rows, gate_vmem[:, cols], preferred_element_type=jnp.float32)
            up_part = jnp.dot(rows, up_vmem[:, cols], preferred_element_type=jnp.float32)
            units = (gate_part / (1.0 + jnp.exp(-gate_part)) * up_part).astype(jnp.bfloat16)
            partial = jnp.dot(units, down_vmem[cols, :], preferred_element_type=jnp.float32)
            if block == 0:
                acc_ref[slot] = partial
            else:
                acc_ref[slot] += partial
    for slot in range(capacity):
        out_ref[:, slot, :] = acc_ref[slot].astype(out_ref.dtype)


def expert_rows(buffer, gate_weight, up_weight, down_weight):
    sources, capacity, model_width = buffer.shape
    hidden_units = gate_weight.shape[-1]
    in_hbm = pl.BlockSpec(memory_space=pl.ANY)
    in_vmem = pl.BlockSpec(memory_space=pltpu.VMEM)
    return pl.pallas_call(
        expert_kernel,
        in_specs=[in_vmem, in_hbm, in_hbm, in_hbm],
        out_specs=in_vmem,
        out_shape=jax.ShapeDtypeStruct(buffer.shape, jnp.bfloat16),
        scratch_shapes=[
            pltpu.VMEM((model_width, hidden_units), jnp.bfloat16),
            pltpu.VMEM((model_width, hidden_units), jnp.bfloat16),
            pltpu.VMEM((hidden_units, model_width), jnp.bfloat16),
            pltpu.VMEM((capacity, sources, model_width), jnp.bfloat16),
            pltpu.VMEM((capacity, sources, model_width), jnp.float32),
            pltpu.SemaphoreType.DMA((3, hidden_units // FF_BLOCK)),
        ],
        compiler_params=pltpu.CompilerParams(vmem_limit_bytes=56 * 1024 * 1024),
    )(buffer, gate_weight, up_weight, down_weight)


def dispatch_kernel(layout_ref, hidden_ref, out_ref):
    hidden_rows = hidden_ref[...]
    for slot in range(out_ref.shape[1]):
        placed = jnp.dot(layout_ref[slot], hidden_rows, preferred_element_type=jnp.float32)
        out_ref[:, slot, :] = placed.astype(out_ref.dtype)


def shards(
    hidden,
    route_ids,
    route_scores,
    gate_weight,
    up_weight,
    down_weight,
    queries,
    latent_cache,
    lengths,
):
    seq_dev, model_width = hidden.shape
    top_count = route_ids.shape[1]
    row_count = lax.axis_size("row")
    col_count = lax.axis_size("col")
    experts = row_count * col_count
    capacity = max(2, 2 * seq_dev * top_count // experts)
    combine = 2.5 * route_scores / jnp.sum(route_scores, axis=-1, keepdims=True)
    flat_ids = route_ids.reshape(-1)
    onehot = (flat_ids[:, None] == jnp.arange(experts, dtype=jnp.int32)[None, :]).astype(jnp.int32)
    before = jnp.cumsum(onehot, axis=0) - onehot
    ranking = jnp.sum(before * onehot, axis=1)
    share = (
        (onehot[None, :, :] > 0)
        & (ranking[None, :, None] == jnp.arange(capacity, dtype=jnp.int32)[:, None, None])
    ).reshape(capacity, seq_dev, top_count, experts)
    layout = jnp.swapaxes(jnp.any(share, axis=2), 1, 2).astype(jnp.bfloat16)
    mixing = jnp.sum(share.astype(jnp.float32) * combine[None, :, :, None], axis=2)
    outgoing = pl.pallas_call(
        dispatch_kernel,
        out_shape=jax.ShapeDtypeStruct((experts, capacity, model_width), jnp.bfloat16),
    )(layout, hidden)
    computed = expert_rows(
        lax.all_to_all(outgoing, ("row", "col"), split_axis=0, concat_axis=0, tiled=True),
        gate_weight,
        up_weight,
        down_weight,
    )
    returned = lax.all_to_all(computed, ("row", "col"), split_axis=0, concat_axis=0, tiled=True)
    mixing = jnp.transpose(mixing, (1, 2, 0)).reshape(seq_dev, experts * capacity)
    returned = returned.reshape(experts * capacity, model_width)
    mixture = jnp.dot(
        mixing,
        returned.astype(jnp.float32),
        precision=lax.Precision.HIGHEST,
        preferred_element_type=jnp.float32,
    ).astype(jnp.bfloat16)
    context = attention(queries, latent_cache, lengths)
    return (mixture, context)


def solution(mesh):
    placed = (
        P(("row", "col"), None),
        P(("row", "col"), None),
        P(("row", "col"), None),
        P(("row", "col"), None, None),
        P(("row", "col"), None, None),
        P(("row", "col"), None, None),
        P(("row", "col"), None, None),
        P(("row", "col"), None, None),
        P(("row", "col")),
    )
    return jax.shard_map(
        shards,
        mesh=mesh,
        in_specs=placed,
        out_specs=(P(("row", "col"), None), P(("row", "col"), None, None)),
        check_vma=False,
    )
```

```python
import jax
import jax.numpy as jnp
from jax import lax
from jax.experimental import pallas as pl
from jax.experimental.pallas import tpu as pltpu
from jax.sharding import PartitionSpec as P

LATENT = 512


SOFTMAX_SCALE = 192 ** (-0.5)


def attention(queries, latent_cache, lengths):
    scores = (
        jnp.einsum("shc,slc->shl", queries, latent_cache, preferred_element_type=jnp.float32)
        * SOFTMAX_SCALE
    )
    visible = (
        jnp.arange(latent_cache.shape[1], dtype=jnp.int32)[None, None, :] < lengths[:, None, None]
    )
    scores = jnp.where(visible, scores, jnp.float32(-1e30))
    row_max = jnp.max(scores, axis=-1, keepdims=True)
    numer = jnp.where(visible, jnp.exp(scores - row_max), jnp.float32(0.0))
    probabilities = (numer / jnp.sum(numer, axis=-1, keepdims=True)).astype(jnp.bfloat16)
    context = jnp.einsum(
        "shl,slc->shc",
        probabilities,
        latent_cache[:, :, :LATENT],
        preferred_element_type=jnp.float32,
    )
    return context.astype(jnp.bfloat16)


FF_BLOCK = 512


def expert_kernel(rows_ref, gate_hbm, up_hbm, down_hbm, out_ref,
                  gate_vmem, up_vmem, down_vmem, slots_ref, acc_ref, sems):
    capacity = rows_ref.shape[1]
    blocks = gate_vmem.shape[-1] // FF_BLOCK
    copies = []
    for block in range(blocks):
        cols = pl.ds(block * FF_BLOCK, FF_BLOCK)
        trio = (
            pltpu.make_async_copy(gate_hbm.at[0, :, cols], gate_vmem.at[:, cols], sems.at[0, block]),
            pltpu.make_async_copy(up_hbm.at[0, :, cols], up_vmem.at[:, cols], sems.at[1, block]),
            pltpu.make_async_copy(down_hbm.at[0, cols, :], down_vmem.at[cols, :], sems.at[2, block]),
        )
        for copy in trio:
            copy.start()
        copies.append(trio)
    for slot in range(capacity):
        slots_ref[slot] = rows_ref[:, slot, :]
    for block in range(blocks):
        cols = pl.ds(block * FF_BLOCK, FF_BLOCK)
        gate_copy, up_copy, down_copy = copies[block]
        gate_copy.wait()
        up_copy.wait()
        down_copy.wait()
        for slot in range(capacity):
            rows = slots_ref[slot]
            gate_part = jnp.dot(rows, gate_vmem[:, cols], preferred_element_type=jnp.float32)
            up_part = jnp.dot(rows, up_vmem[:, cols], preferred_element_type=jnp.float32)
            units = (gate_part / (1.0 + jnp.exp(-gate_part)) * up_part).astype(jnp.bfloat16)
            partial = jnp.dot(units, down_vmem[cols, :], preferred_element_type=jnp.float32)
            if block == 0:
                acc_ref[slot] = partial
            else:
                acc_ref[slot] += partial
    for slot in range(capacity):
        out_ref[:, slot, :] = acc_ref[slot].astype(out_ref.dtype)


def expert_rows(buffer, gate_weight, up_weight, down_weight):
    sources, capacity, model_width = buffer.shape
    hidden_units = gate_weight.shape[-1]
    in_hbm = pl.BlockSpec(memory_space=pl.ANY)
    in_vmem = pl.BlockSpec(memory_space=pltpu.VMEM)
    return pl.pallas_call(
        expert_kernel,
        in_specs=[in_vmem, in_hbm, in_hbm, in_hbm],
        out_specs=in_vmem,
        out_shape=jax.ShapeDtypeStruct(buffer.shape, jnp.bfloat16),
        scratch_shapes=[
            pltpu.VMEM((model_width, hidden_units), jnp.bfloat16),
            pltpu.VMEM((model_width, hidden_units), jnp.bfloat16),
            pltpu.VMEM((hidden_units, model_width), jnp.bfloat16),
            pltpu.VMEM((capacity, sources, model_width), jnp.bfloat16),
            pltpu.VMEM((capacity, sources, model_width), jnp.float32),
            pltpu.SemaphoreType.DMA((3, hidden_units // FF_BLOCK)),
        ],
        compiler_params=pltpu.CompilerParams(vmem_limit_bytes=56 * 1024 * 1024),
    )(buffer, gate_weight, up_weight, down_weight)


def dispatch_kernel(layout_ref, hidden_ref, out_ref):
    hidden_rows = hidden_ref[...]
    for slot in range(out_ref.shape[1]):
        placed = jnp.dot(layout_ref[slot], hidden_rows, preferred_element_type=jnp.float32)
        out_ref[:, slot, :] = placed.astype(out_ref.dtype)


def shards(
    hidden,
    route_ids,
    route_scores,
    gate_weight,
    up_weight,
    down_weight,
    queries,
    latent_cache,
    lengths,
):
    seq_dev, model_width = hidden.shape
    top_count = route_ids.shape[1]
    row_count = lax.axis_size("row")
    col_count = lax.axis_size("col")
    experts = row_count * col_count
    capacity = max(2, 2 * seq_dev * top_count // experts)
    combine = 2.5 * route_scores / jnp.sum(route_scores, axis=-1, keepdims=True)
    flat_ids = route_ids.reshape(-1)
    onehot = (flat_ids[:, None] == jnp.arange(experts, dtype=jnp.int32)[None, :]).astype(jnp.int32)
    before = jnp.cumsum(onehot, axis=0) - onehot
    ranking = jnp.sum(before * onehot, axis=1)
    share = (
        (onehot[None, :, :] > 0)
        & (ranking[None, :, None] == jnp.arange(capacity, dtype=jnp.int32)[:, None, None])
    ).reshape(capacity, seq_dev, top_count, experts)
    layout = jnp.swapaxes(jnp.any(share, axis=2), 1, 2).astype(jnp.bfloat16)
    mixing = jnp.sum(share.astype(jnp.float32) * combine[None, :, :, None], axis=2)
    outgoing = pl.pallas_call(
        dispatch_kernel,
        out_shape=jax.ShapeDtypeStruct((experts, capacity, model_width), jnp.bfloat16),
    )(layout, hidden)
    context = attention(queries, latent_cache, lengths)
    received = lax.all_to_all(outgoing, ("row", "col"), split_axis=0, concat_axis=0, tiled=True)
    context, received = lax.optimization_barrier((context, received))
    computed = expert_rows(received, gate_weight, up_weight, down_weight)
    returned = lax.all_to_all(computed, ("row", "col"), split_axis=0, concat_axis=0, tiled=True)
    mixing = jnp.transpose(mixing, (1, 2, 0)).reshape(seq_dev, experts * capacity)
    returned = returned.reshape(experts * capacity, model_width)
    mixture = jnp.dot(
        mixing,
        returned.astype(jnp.float32),
        precision=lax.Precision.HIGHEST,
        preferred_element_type=jnp.float32,
    ).astype(jnp.bfloat16)
    return (mixture, context)


def solution(mesh):
    placed = (
        P(("row", "col"), None),
        P(("row", "col"), None),
        P(("row", "col"), None),
        P(("row", "col"), None, None),
        P(("row", "col"), None, None),
        P(("row", "col"), None, None),
        P(("row", "col"), None, None),
        P(("row", "col"), None, None),
        P(("row", "col")),
    )
    return jax.shard_map(
        shards,
        mesh=mesh,
        in_specs=placed,
        out_specs=(P(("row", "col"), None), P(("row", "col"), None, None)),
        check_vma=False,
    )
```

```python
import jax
import jax.numpy as jnp
from jax import lax
from jax.experimental import pallas as pl
from jax.experimental.pallas import tpu as pltpu
from jax.sharding import PartitionSpec as P

LATENT = 512


SOFTMAX_SCALE = 192 ** (-0.5)


def attention(queries, latent_cache, lengths):
    scores = (
        jnp.einsum("shc,slc->shl", queries, latent_cache, preferred_element_type=jnp.float32)
        * SOFTMAX_SCALE
    )
    visible = (
        jnp.arange(latent_cache.shape[1], dtype=jnp.int32)[None, None, :] < lengths[:, None, None]
    )
    scores = jnp.where(visible, scores, jnp.float32(-1e30))
    row_max = jnp.max(scores, axis=-1, keepdims=True)
    numer = jnp.where(visible, jnp.exp(scores - row_max), jnp.float32(0.0))
    probabilities = (numer / jnp.sum(numer, axis=-1, keepdims=True)).astype(jnp.bfloat16)
    context = jnp.einsum(
        "shl,slc->shc",
        probabilities,
        latent_cache[:, :, :LATENT],
        preferred_element_type=jnp.float32,
    )
    return context.astype(jnp.bfloat16)


FF_BLOCKS = (512, 512)
LOOKAHEAD = 1


def expert_kernel(rows_ref, gate_hbm, up_hbm, down_hbm, out_ref,
                  gate_vmem, up_vmem, down_vmem, slots_ref, acc_ref, sems):
    capacity = rows_ref.shape[1]
    bounds = [0]
    for width in FF_BLOCKS:
        bounds.append(bounds[-1] + width)
    spans = [pl.ds(low, high - low) for low, high in zip(bounds[:-1], bounds[1:])]
    copies = []
    for block, cols in enumerate(spans):
        copies.append((
            pltpu.make_async_copy(gate_hbm.at[0, :, cols], gate_vmem.at[:, cols], sems.at[0, block]),
            pltpu.make_async_copy(up_hbm.at[0, :, cols], up_vmem.at[:, cols], sems.at[1, block]),
            pltpu.make_async_copy(down_hbm.at[0, cols, :], down_vmem.at[cols, :], sems.at[2, block]),
        ))
    for block in range(min(LOOKAHEAD, len(spans))):
        for copy in copies[block]:
            copy.start()
    for slot in range(capacity):
        slots_ref[slot] = rows_ref[:, slot, :]
    for block, cols in enumerate(spans):
        gate_copy, up_copy, down_copy = copies[block]
        gate_copy.wait()
        up_copy.wait()
        down_copy.wait()
        if block + LOOKAHEAD < len(spans):
            for copy in copies[block + LOOKAHEAD]:
                copy.start()
        for slot in range(capacity):
            rows = slots_ref[slot]
            gate_part = jnp.dot(rows, gate_vmem[:, cols], preferred_element_type=jnp.float32)
            up_part = jnp.dot(rows, up_vmem[:, cols], preferred_element_type=jnp.float32)
            units = (gate_part / (1.0 + jnp.exp(-gate_part)) * up_part).astype(jnp.bfloat16)
            partial = jnp.dot(units, down_vmem[cols, :], preferred_element_type=jnp.float32)
            if block == 0:
                acc_ref[slot] = partial
            else:
                acc_ref[slot] += partial
    for slot in range(capacity):
        out_ref[:, slot, :] = acc_ref[slot].astype(out_ref.dtype)


def expert_rows(buffer, gate_weight, up_weight, down_weight):
    sources, capacity, model_width = buffer.shape
    hidden_units = gate_weight.shape[-1]
    in_hbm = pl.BlockSpec(memory_space=pl.ANY)
    in_vmem = pl.BlockSpec(memory_space=pltpu.VMEM)
    return pl.pallas_call(
        expert_kernel,
        in_specs=[in_vmem, in_hbm, in_hbm, in_hbm],
        out_specs=in_vmem,
        out_shape=jax.ShapeDtypeStruct(buffer.shape, jnp.bfloat16),
        scratch_shapes=[
            pltpu.VMEM((model_width, hidden_units), jnp.bfloat16),
            pltpu.VMEM((model_width, hidden_units), jnp.bfloat16),
            pltpu.VMEM((hidden_units, model_width), jnp.bfloat16),
            pltpu.VMEM((capacity, sources, model_width), jnp.bfloat16),
            pltpu.VMEM((capacity, sources, model_width), jnp.float32),
            pltpu.SemaphoreType.DMA((3, len(FF_BLOCKS))),
        ],
        compiler_params=pltpu.CompilerParams(vmem_limit_bytes=56 * 1024 * 1024),
    )(buffer, gate_weight, up_weight, down_weight)


def dispatch_kernel(layout_ref, hidden_ref, out_ref):
    hidden_rows = hidden_ref[...]
    for slot in range(out_ref.shape[1]):
        placed = lax.dot_general(
            layout_ref[slot], hidden_rows, (((0,), (0,)), ((), ())),
            preferred_element_type=jnp.float32,
        )
        out_ref[:, slot, :] = placed.astype(out_ref.dtype)


def shards(
    hidden,
    route_ids,
    route_scores,
    gate_weight,
    up_weight,
    down_weight,
    queries,
    latent_cache,
    lengths,
):
    seq_dev, model_width = hidden.shape
    top_count = route_ids.shape[1]
    row_count = lax.axis_size("row")
    col_count = lax.axis_size("col")
    experts = row_count * col_count
    capacity = max(2, 2 * seq_dev * top_count // experts)
    combine = 2.5 * route_scores / jnp.sum(route_scores, axis=-1, keepdims=True)
    flat_ids = route_ids.reshape(-1)
    onehot = (flat_ids[:, None] == jnp.arange(experts, dtype=jnp.int32)[None, :]).astype(jnp.int32)
    before = jnp.cumsum(onehot, axis=0) - onehot
    ranking = jnp.sum(before * onehot, axis=1)
    share = (
        (onehot[None, :, :] > 0)
        & (ranking[None, :, None] == jnp.arange(capacity, dtype=jnp.int32)[:, None, None])
    ).reshape(capacity, seq_dev, top_count, experts)
    layout = jnp.any(share, axis=2).astype(jnp.bfloat16)
    mixing = jnp.sum(share.astype(jnp.float32) * combine[None, :, :, None], axis=2)
    outgoing = pl.pallas_call(
        dispatch_kernel,
        out_shape=jax.ShapeDtypeStruct((experts, capacity, model_width), jnp.bfloat16),
    )(layout, hidden)
    computed = expert_rows(
        lax.all_to_all(outgoing, ("row", "col"), split_axis=0, concat_axis=0, tiled=True),
        gate_weight,
        up_weight,
        down_weight,
    )
    returned = lax.all_to_all(computed, ("row", "col"), split_axis=0, concat_axis=0, tiled=True)
    mixing = jnp.transpose(mixing, (1, 2, 0)).reshape(seq_dev, experts * capacity)
    returned = returned.reshape(experts * capacity, model_width)
    mixture = jnp.dot(
        mixing,
        returned.astype(jnp.float32),
        precision=lax.Precision.HIGHEST,
        preferred_element_type=jnp.float32,
    ).astype(jnp.bfloat16)
    context = attention(queries, latent_cache, lengths)
    return (mixture, context)


def solution(mesh):
    placed = (
        P(("row", "col"), None),
        P(("row", "col"), None),
        P(("row", "col"), None),
        P(("row", "col"), None, None),
        P(("row", "col"), None, None),
        P(("row", "col"), None, None),
        P(("row", "col"), None, None),
        P(("row", "col"), None, None),
        P(("row", "col")),
    )
    return jax.shard_map(
        shards,
        mesh=mesh,
        in_specs=placed,
        out_specs=(P(("row", "col"), None), P(("row", "col"), None, None)),
        check_vma=False,
    )
```

```python
import jax
import jax.numpy as jnp
from jax import lax
from jax.experimental import pallas as pl
from jax.experimental.pallas import tpu as pltpu
from jax.sharding import PartitionSpec as P

LATENT = 512


SOFTMAX_SCALE = 192 ** (-0.5)


def attention(queries, latent_cache, lengths):
    scores = (
        jnp.einsum("shc,slc->shl", queries, latent_cache, preferred_element_type=jnp.float32)
        * SOFTMAX_SCALE
    )
    visible = (
        jnp.arange(latent_cache.shape[1], dtype=jnp.int32)[None, None, :] < lengths[:, None, None]
    )
    scores = jnp.where(visible, scores, jnp.float32(-1e30))
    row_max = jnp.max(scores, axis=-1, keepdims=True)
    numer = jnp.where(visible, jnp.exp(scores - row_max), jnp.float32(0.0))
    probabilities = (numer / jnp.sum(numer, axis=-1, keepdims=True)).astype(jnp.bfloat16)
    context = jnp.einsum(
        "shl,slc->shc",
        probabilities,
        latent_cache[:, :, :LATENT],
        preferred_element_type=jnp.float32,
    )
    return context.astype(jnp.bfloat16)


FF_BLOCK = 512


def expert_kernel(rows_ref, gate_hbm, up_hbm, down_hbm, out_ref,
                  gate_vmem, up_vmem, down_vmem, slots_ref, acc_ref, sems):
    capacity = rows_ref.shape[1]
    blocks = gate_vmem.shape[-1] // FF_BLOCK
    copies = []
    for block in range(blocks):
        cols = pl.ds(block * FF_BLOCK, FF_BLOCK)
        trio = (
            pltpu.make_async_copy(gate_hbm.at[0, :, cols], gate_vmem.at[:, cols], sems.at[0, block]),
            pltpu.make_async_copy(up_hbm.at[0, :, cols], up_vmem.at[:, cols], sems.at[1, block]),
            pltpu.make_async_copy(down_hbm.at[0, cols, :], down_vmem.at[cols, :], sems.at[2, block]),
        )
        for copy in trio:
            copy.start()
        copies.append(trio)
    for slot in range(capacity):
        slots_ref[slot] = rows_ref[:, slot, :]
    for block in range(blocks):
        cols = pl.ds(block * FF_BLOCK, FF_BLOCK)
        gate_copy, up_copy, down_copy = copies[block]
        gate_copy.wait()
        up_copy.wait()
        down_copy.wait()
        for slot in range(capacity):
            rows = slots_ref[slot]
            gate_part = jnp.dot(rows, gate_vmem[:, cols], preferred_element_type=jnp.float32)
            up_part = jnp.dot(rows, up_vmem[:, cols], preferred_element_type=jnp.float32)
            units = (gate_part / (1.0 + jnp.exp(-gate_part)) * up_part).astype(jnp.bfloat16)
            partial = jnp.dot(units, down_vmem[cols, :], preferred_element_type=jnp.float32)
            if block == 0:
                acc_ref[slot] = partial
            else:
                acc_ref[slot] += partial
    for slot in range(capacity):
        out_ref[:, slot, :] = acc_ref[slot].astype(out_ref.dtype)


def expert_rows(buffer, gate_weight, up_weight, down_weight):
    sources, capacity, model_width = buffer.shape
    hidden_units = gate_weight.shape[-1]
    in_hbm = pl.BlockSpec(memory_space=pl.ANY)
    in_vmem = pl.BlockSpec(memory_space=pltpu.VMEM)
    return pl.pallas_call(
        expert_kernel,
        in_specs=[in_vmem, in_hbm, in_hbm, in_hbm],
        out_specs=in_vmem,
        out_shape=jax.ShapeDtypeStruct(buffer.shape, jnp.bfloat16),
        scratch_shapes=[
            pltpu.VMEM((model_width, hidden_units), jnp.bfloat16),
            pltpu.VMEM((model_width, hidden_units), jnp.bfloat16),
            pltpu.VMEM((hidden_units, model_width), jnp.bfloat16),
            pltpu.VMEM((capacity, sources, model_width), jnp.bfloat16),
            pltpu.VMEM((capacity, sources, model_width), jnp.float32),
            pltpu.SemaphoreType.DMA((3, hidden_units // FF_BLOCK)),
        ],
        compiler_params=pltpu.CompilerParams(vmem_limit_bytes=56 * 1024 * 1024),
    )(buffer, gate_weight, up_weight, down_weight)


def dispatch_kernel(layout_ref, hidden_ref, out_ref):
    hidden_rows = hidden_ref[...]
    for slot in range(out_ref.shape[1]):
        placed = lax.dot_general(
            layout_ref[slot], hidden_rows, (((0,), (0,)), ((), ())),
            preferred_element_type=jnp.float32,
        )
        out_ref[:, slot, :] = placed.astype(out_ref.dtype)


def shards(
    hidden,
    route_ids,
    route_scores,
    gate_weight,
    up_weight,
    down_weight,
    queries,
    latent_cache,
    lengths,
):
    seq_dev, model_width = hidden.shape
    top_count = route_ids.shape[1]
    row_count = lax.axis_size("row")
    col_count = lax.axis_size("col")
    experts = row_count * col_count
    capacity = max(2, 2 * seq_dev * top_count // experts)
    combine = 2.5 * route_scores / jnp.sum(route_scores, axis=-1, keepdims=True)
    flat_ids = route_ids.reshape(-1)
    onehot = (flat_ids[:, None] == jnp.arange(experts, dtype=jnp.int32)[None, :]).astype(jnp.int32)
    before = jnp.cumsum(onehot, axis=0) - onehot
    ranking = jnp.sum(before * onehot, axis=1)
    share = (
        (onehot[None, :, :] > 0)
        & (ranking[None, :, None] == jnp.arange(capacity, dtype=jnp.int32)[:, None, None])
    ).reshape(capacity, seq_dev, top_count, experts)
    layout = jnp.any(share, axis=2).astype(jnp.bfloat16)
    mixing = jnp.sum(share.astype(jnp.float32) * combine[None, :, :, None], axis=2)
    outgoing = pl.pallas_call(
        dispatch_kernel,
        out_shape=jax.ShapeDtypeStruct((experts, capacity, model_width), jnp.bfloat16),
    )(layout, hidden)
    computed = expert_rows(
        lax.all_to_all(outgoing, ("row", "col"), split_axis=0, concat_axis=0, tiled=True),
        gate_weight,
        up_weight,
        down_weight,
    )
    returned = lax.all_to_all(computed, ("row", "col"), split_axis=0, concat_axis=0, tiled=True)
    mixing = jnp.transpose(mixing, (1, 2, 0)).reshape(seq_dev, experts * capacity)
    returned = returned.reshape(experts * capacity, model_width)
    mixture = jnp.dot(
        mixing,
        returned.astype(jnp.float32),
        precision=lax.Precision.HIGHEST,
        preferred_element_type=jnp.float32,
    ).astype(jnp.bfloat16)
    context = attention(queries, latent_cache, lengths)
    return (mixture, context)


def solution(mesh):
    placed = (
        P(("row", "col"), None),
        P(("row", "col"), None),
        P(("row", "col"), None),
        P(("row", "col"), None, None),
        P(("row", "col"), None, None),
        P(("row", "col"), None, None),
        P(("row", "col"), None, None),
        P(("row", "col"), None, None),
        P(("row", "col")),
    )
    return jax.shard_map(
        shards,
        mesh=mesh,
        in_specs=placed,
        out_specs=(P(("row", "col"), None), P(("row", "col"), None, None)),
        check_vma=False,
    )
```
